512 devices in a mesh: segment: 8 (over y_hi, x), dp: 64 (over y_lo, z, core).
Axes of the slice: x: 4, y: 4 (y_hi: 2, y_lo: 2; y = y_hi * 2 + y_lo), z: 16, core: 2. Of those that a mesh axis runs over, the one named last changes fastest.
Arguments:
- acts: bfloat16 [8, 128, 4, 8, 8, 128], P('segment', 'dp'), may hold values from -6 to 6
- weights: bfloat16 [8, 3456, 128], P('segment', 'dp'), may hold values from -0.109375 to 0.109375
- pos_weight: float32 [8, 3, 128], P('segment'), may hold values from -4 to 4
- anchors: int32 [128, 3], P('dp'), may hold values from 0 to 1983
- top_grad: bfloat16 [128, 4, 8, 8, 128], P('dp'), may hold values from -6 to 6
Outputs:
- section_grads: bfloat16 [8, 128, 4, 8, 8, 128], P('segment', 'dp')
- weight_grad: float32 [8, 3456, 128], P('segment', 'dp')
The draws below stay inside these ranges and needn't reach their ends.
Inputs may be any that keep to these rules, and one draw needn't show every extreme that they name: `anchors`: mesh coordinates of each crop's corner.
All inputs are finite; a program needn't handle non-finite values.
Results may differ from the reference program's by a relative error of at most 0.015.
Values may be sent and summed in bfloat16 or wider, within the bound.
No kernel may reach another device: no remote copies, remote signals or barrier semaphores. Data moves between devices by JAX's collectives and lax.ppermute only.
A program may use at most 64 MiB of HBM per device.

```python
import math
import jax
import jax.numpy as jnp
from jax import lax

C = 128
KV = 27
PX = 4
PY = 8
PZ = 8
STRIDE = 2
WAVE = 64
SEGMENTS = 8
BATCH = 128
ROWS = 3456
CELLS_ALL = 32768


def with_ends(drawn, key, smallest, top_value):
    shape = drawn.shape
    spot = [jax.random.randint(jax.random.fold_in(key, axis), (), 0, shape[axis]) for axis in range(len(shape))]
    drawn = drawn.at[tuple(spot)].set(smallest)
    longest = shape.index(max(shape))
    spot[longest] = (spot[longest] + 1) % shape[longest]
    return drawn.at[tuple(spot)].set(top_value)


def block_levels(stream_key, shape, pieces, least, high):
    level = 1.0
    for axis_at, shards_of in pieces:
        steps = jax.random.uniform(jax.random.fold_in(jax.random.fold_in(stream_key, 6), axis_at), (shards_of,), jnp.float32, least / len(pieces), high / len(pieces))
        level = level * jnp.repeat(jnp.exp(steps), shape[axis_at] // shards_of).reshape((-1,) + (1,) * (len(shape) - 1 - axis_at))
    return level


def gaussian(rng, dims, width, reach, pieces=(), kind=jnp.bfloat16):
    factor_of = block_levels(rng, dims, pieces, -0.22, 0.18) if pieces else 1.0
    drawn = jax.random.normal(rng, dims, jnp.float32) * width * factor_of
    return jnp.minimum(jnp.maximum(drawn, -reach), reach).astype(kind)


def setup_inputs(seed: int = 0) -> dict:
    key_list = jax.random.split(jax.random.key(seed), 6)
    return {
        "acts": gaussian(key_list[0], (SEGMENTS, BATCH, PX, PY, PZ, C), 1.0, 6.0, ((0, 8), (1, 64))),
        "weights": gaussian(key_list[1], (SEGMENTS, ROWS, C), (KV * C) ** -0.5, 0.109375, ((0, 8), (1, 64))),
        "pos_weight": gaussian(key_list[2], (SEGMENTS, 3, C), 0.7, 4.0, ((0, 8),), jnp.float32),
        "anchors": with_ends(jax.random.randint(key_list[3], (BATCH, 3), 0, 1984), jax.random.fold_in(key_list[3], 1), 0, 1983).astype(jnp.int32),
        "top_grad": gaussian(key_list[4], (BATCH, PX, PY, PZ, C), 1.0, 6.0, ((0, 64),)),
    }


def apply_taps(field, kernel_taps):
    size_x, size_y, size_z, channels = field.shape
    padded = jnp.pad(field, ((1, 1), (1, 1), (1, 1), (0, 0)))
    summed = jnp.zeros((size_x * size_y * size_z, kernel_taps.shape[2]), jnp.float32)
    tap_index = 0
    for first in range(3):
        for second in range(3):
            for third in range(3):
                window_rows = padded[first:first + size_x, second:second + size_y, third:third + size_z].reshape(size_x * size_y * size_z, channels)
                summed = summed + jnp.dot(window_rows, kernel_taps[tap_index], preferred_element_type=jnp.float32)
                tap_index += 1
    return summed

def tap_grads(field, slope):
    size_x, size_y, size_z, channels = field.shape
    padded = jnp.pad(field, ((1, 1), (1, 1), (1, 1), (0, 0)))
    blocks = []
    for first in range(3):
        for second in range(3):
            for third in range(3):
                window_rows = padded[first:first + size_x, second:second + size_y, third:third + size_z].reshape(size_x * size_y * size_z, channels)
                blocks.append(jnp.dot(window_rows.T, slope, preferred_element_type=jnp.float32))
    return jnp.concatenate(blocks, axis=0)

def position_term(anchor, pos_gain, size_x, size_y, size_z):
    phases = []
    for axis_num, axis_len in enumerate((size_x, size_y, size_z)):
        coords = anchor[axis_num] + STRIDE * jnp.arange(axis_len, dtype=jnp.int32)
        phase_val = (coords % WAVE).astype(jnp.float32)
        phases.append(jnp.sin(phase_val * (2.0 * math.pi / WAVE)))
    position_sum = phases[0][:, None, None, None] * pos_gain[0] + phases[1][None, :, None, None] * pos_gain[1] + phases[2][None, None, :, None] * pos_gain[2]
    return position_sum.reshape(size_x * size_y * size_z, pos_gain.shape[1])

def layer_slope(incoming_rows, pre_act):
    sigmoid_h = jax.nn.sigmoid(pre_act)
    silu_slope = sigmoid_h * (1.0 + pre_act * (1.0 - sigmoid_h))
    return (incoming_rows * silu_slope).astype(jnp.bfloat16)

def reference(acts, weights, pos_weight, anchors, top_grad):
    cell_count = PX * PY * PZ
    scale_factor = 1.0 / math.sqrt(CELLS_ALL)
    cotangent = top_grad
    grads_out = [None] * SEGMENTS
    wgrads_out = [None] * SEGMENTS
    for segment_num in range(SEGMENTS - 1, -1, -1):
        kernel_taps = weights[segment_num].reshape(KV, C, C)
        flipped = jnp.transpose(jnp.flip(kernel_taps, 0), (0, 2, 1))
        pos_gain = pos_weight[segment_num]

        def one_item(carry, item, kernel_taps=kernel_taps, flipped=flipped, pos_gain=pos_gain):
            field, incoming, anchor = item
            pre_act = apply_taps(field, kernel_taps) + position_term(anchor, pos_gain, PX, PY, PZ)
            incoming_rows = incoming.reshape(cell_count, C).astype(jnp.float32)
            slope = layer_slope(incoming_rows, pre_act)
            down_grad = (incoming_rows + apply_taps(slope.reshape(PX, PY, PZ, C), flipped)).astype(jnp.bfloat16)
            return (carry + tap_grads(field, slope), down_grad.reshape(PX, PY, PZ, C))
        summed, cotangent = lax.scan(one_item, jnp.zeros((KV * C, C), jnp.float32), (acts[segment_num], cotangent, anchors))
        grads_out[segment_num] = cotangent
        wgrads_out[segment_num] = summed * scale_factor
    return (jnp.stack(grads_out), jnp.stack(wgrads_out))
```

```python
import math

import jax
import jax.numpy as jnp
from jax import lax
from jax.sharding import PartitionSpec as P

STRIDE = 2
WAVE = 64


def passed_along(array, axis, by):
    length = lax.axis_size(axis)
    pairs = [(i, i + by) for i in range(length) if 0 <= i + by < length]
    return lax.ppermute(array, axis, pairs)


def conv_forward(field, kernel):
    return lax.conv_general_dilated(
        field, kernel, (1, 1, 1), [(1, 1)] * 3,
        dimension_numbers=("NDHWC", "DHWIO", "NDHWC"),
        preferred_element_type=jnp.float32,
    )


def conv_transposed(slope, kernel):
    flipped = jnp.flip(kernel, (0, 1, 2))
    return lax.conv_general_dilated(
        slope, flipped, (1, 1, 1), [(1, 1)] * 3,
        dimension_numbers=("NDHWC", "DHWOI", "NDHWC"),
        preferred_element_type=jnp.float32,
    )


def conv_kernel_grad(field, slope):
    return lax.conv_general_dilated(
        field, slope, (1, 1, 1), [(1, 1)] * 3,
        dimension_numbers=("CDHWN", "IDHWO", "DHWNC"),
        preferred_element_type=jnp.float32,
    )


def position_term(anchor, pos_gain, size_x, size_y, size_z):
    phases = []
    for axis_num, axis_len in enumerate((size_x, size_y, size_z)):
        coords = anchor[axis_num] + STRIDE * jnp.arange(axis_len, dtype=jnp.int32)
        phase_val = (coords % WAVE).astype(jnp.float32)
        phases.append(jnp.sin(phase_val * (2.0 * math.pi / WAVE)))
    return (
        phases[0][:, None, None, None] * pos_gain[0]
        + phases[1][None, :, None, None] * pos_gain[1]
        + phases[2][None, None, :, None] * pos_gain[2]
    )


def local(acts, weights, pos_weight, anchors, top_grad):
    segments = lax.axis_size("segment")
    dp_count = lax.axis_size("dp")
    segment_index = lax.axis_index("segment")
    channels = weights.shape[2]
    gathered = lax.all_gather(weights, "dp", axis=0, tiled=True)
    kernel = gathered.reshape(3, 3, 3, channels, channels)
    fields = acts[0]
    micro_count, size_x, size_y, size_z = fields.shape[:4]
    cell_count = size_x * size_y * size_z
    pos_gain = pos_weight[0]
    position_all = jnp.stack(
        [position_term(anchors[m], pos_gain, size_x, size_y, size_z) for m in range(micro_count)]
    )
    pre_act = conv_forward(fields, kernel) + position_all
    sigmoid_h = jax.nn.sigmoid(pre_act)
    silu_slope = sigmoid_h * (1.0 + pre_act * (1.0 - sigmoid_h))

    is_top = segment_index == segments - 1
    incoming = jnp.zeros(top_grad.shape, jnp.bfloat16)
    grads_held = jnp.zeros(top_grad.shape, jnp.bfloat16)
    slope_held = jnp.zeros(top_grad.shape, jnp.bfloat16)
    for tick in range(segments):
        cotangent = jnp.where(is_top, top_grad, incoming).astype(jnp.float32)
        slope = (cotangent * silu_slope).astype(jnp.bfloat16)
        down_grad = (cotangent + conv_transposed(slope, kernel)).astype(jnp.bfloat16)
        mine = segment_index == segments - 1 - tick
        grads_held = jnp.where(mine, down_grad, grads_held)
        slope_held = jnp.where(mine, slope, slope_held)
        if tick + 1 < segments:
            incoming = passed_along(down_grad, "segment", -1)

    grad_term = conv_kernel_grad(fields, slope_held).reshape(dp_count, -1, channels)
    reduced = lax.psum_scatter(grad_term, "dp", scatter_dimension=0, tiled=True)
    scale_factor = 1.0 / math.sqrt(dp_count * micro_count * cell_count)
    return (grads_held[None], reduced * scale_factor)


def solution(mesh):
    return jax.shard_map(
        local,
        mesh=mesh,
        in_specs=(
            P("segment", "dp", None, None, None, None),
            P("segment", "dp", None),
            P("segment", None, None),
            P("dp", None),
            P("dp", None, None, None, None),
        ),
        out_specs=(P("segment", "dp", None, None, None, None), P("segment", "dp", None)),
        check_vma=False,
    )
```

```python
import math

import jax
import jax.numpy as jnp
from jax import lax
from jax.sharding import PartitionSpec as P

STRIDE = 2
WAVE = 64


def passed_along(array, axis, by):
    length = lax.axis_size(axis)
    pairs = [(i, i + by) for i in range(length) if 0 <= i + by < length]
    return lax.ppermute(array, axis, pairs)


def exchanged(array, axis, mask):
    length = lax.axis_size(axis)
    return lax.ppermute(array, axis, [(i, i ^ mask) for i in range(length)])


def bit_count(length):
    return length.bit_length() - 1


def gather_by_halves(block, axis, order):
    index = lax.axis_index(axis)
    held = block
    for bit in order:
        upper = ((index >> bit) & 1) == 1
        received = exchanged(held, axis, 1 << bit)
        low = jnp.where(upper, received, held)
        high = jnp.where(upper, held, received)
        held = jnp.stack([low, high])
    done = len(order)
    natural = [done - 1 - order.index(bit) for bit in range(done - 1, -1, -1)]
    held = jnp.transpose(held, natural + list(range(done, held.ndim)))
    return held.reshape((-1,) + block.shape[1:])


def reduce_by_halves(chunks, axis, order):
    index = lax.axis_index(axis)
    done = len(order)
    held = chunks.reshape((2,) * done + chunks.shape[1:])
    held = jnp.transpose(held, [done - 1 - bit for bit in order] + list(range(done, held.ndim)))
    for bit in order:
        mine = (index >> bit) & 1
        kept = lax.dynamic_index_in_dim(held, mine, 0, keepdims=False)
        sent = lax.dynamic_index_in_dim(held, 1 - mine, 0, keepdims=False)
        held = kept + exchanged(sent, axis, 1 << bit)
    return held.reshape((1,) + chunks.shape[1:])


def conv_forward(field, kernel):
    return lax.conv_general_dilated(
        field, kernel, (1, 1, 1), [(1, 1)] * 3,
        dimension_numbers=("NDHWC", "DHWIO", "NDHWC"),
        preferred_element_type=jnp.float32,
    )


def conv_transposed(slope, kernel):
    flipped = jnp.flip(kernel, (0, 1, 2))
    return lax.conv_general_dilated(
        slope, flipped, (1, 1, 1), [(1, 1)] * 3,
        dimension_numbers=("NDHWC", "DHWOI", "NDHWC"),
        preferred_element_type=jnp.float32,
    )


def conv_kernel_grad(field, slope):
    return lax.conv_general_dilated(
        field, slope, (1, 1, 1), [(1, 1)] * 3,
        dimension_numbers=("CDHWN", "IDHWO", "DHWNC"),
        preferred_element_type=jnp.float32,
    )


def position_term(anchor, pos_gain, size_x, size_y, size_z):
    phases = []
    for axis_num, axis_len in enumerate((size_x, size_y, size_z)):
        coords = anchor[axis_num] + STRIDE * jnp.arange(axis_len, dtype=jnp.int32)
        phase_val = (coords % WAVE).astype(jnp.float32)
        phases.append(jnp.sin(phase_val * (2.0 * math.pi / WAVE)))
    return (
        phases[0][:, None, None, None] * pos_gain[0]
        + phases[1][None, :, None, None] * pos_gain[1]
        + phases[2][None, None, :, None] * pos_gain[2]
    )


def local(acts, weights, pos_weight, anchors, top_grad):
    segments = lax.axis_size("segment")
    dp_count = lax.axis_size("dp")
    segment_index = lax.axis_index("segment")
    channels = weights.shape[2]
    bits = bit_count(dp_count)
    gather_order = list(range(bits - 1, -1, -1))
    gathered = gather_by_halves(weights[0][None], "dp", gather_order)
    kernel = gathered.reshape(3, 3, 3, channels, channels)
    fields = acts[0]
    micro_count, size_x, size_y, size_z = fields.shape[:4]
    cell_count = size_x * size_y * size_z
    pos_gain = pos_weight[0]
    position_all = jnp.stack(
        [position_term(anchors[m], pos_gain, size_x, size_y, size_z) for m in range(micro_count)]
    )
    pre_act = conv_forward(fields, kernel) + position_all
    sigmoid_h = jax.nn.sigmoid(pre_act)
    silu_slope = sigmoid_h * (1.0 + pre_act * (1.0 - sigmoid_h))

    is_top = segment_index == segments - 1
    incoming = jnp.zeros(top_grad.shape, jnp.bfloat16)
    grads_held = jnp.zeros(top_grad.shape, jnp.bfloat16)
    slope_held = jnp.zeros(top_grad.shape, jnp.bfloat16)
    for tick in range(segments):
        cotangent = jnp.where(is_top, top_grad, incoming).astype(jnp.float32)
        slope = (cotangent * silu_slope).astype(jnp.bfloat16)
        down_grad = (cotangent + conv_transposed(slope, kernel)).astype(jnp.bfloat16)
        mine = segment_index == segments - 1 - tick
        grads_held = jnp.where(mine, down_grad, grads_held)
        slope_held = jnp.where(mine, slope, slope_held)
        if tick + 1 < segments:
            incoming = passed_along(down_grad, "segment", -1)

    grad_term = conv_kernel_grad(fields, slope_held).reshape(dp_count, -1, channels)
    reduced = reduce_by_halves(grad_term, "dp", list(range(bits)))
    scale_factor = 1.0 / math.sqrt(dp_count * micro_count * cell_count)
    return (grads_held[None], reduced * scale_factor)


def solution(mesh):
    return jax.shard_map(
        local,
        mesh=mesh,
        in_specs=(
            P("segment", "dp", None, None, None, None),
            P("segment", "dp", None),
            P("segment", None, None),
            P("dp", None),
            P("dp", None, None, None, None),
        ),
        out_specs=(P("segment", "dp", None, None, None, None), P("segment", "dp", None)),
        check_vma=False,
    )
```

```python
import math

import jax
import jax.numpy as jnp
from jax import lax
from jax.sharding import PartitionSpec as P

STRIDE = 2
WAVE = 64


def passed_along(array, axis, by):
    length = lax.axis_size(axis)
    pairs = [(i, i + by) for i in range(length) if 0 <= i + by < length]
    return lax.ppermute(array, axis, pairs)


def exchanged(array, axis, mask):
    length = lax.axis_size(axis)
    return lax.ppermute(array, axis, [(i, i ^ mask) for i in range(length)])


def bit_count(length):
    return length.bit_length() - 1


def gather_by_halves(block, axis, order):
    index = lax.axis_index(axis)
    held = block
    for bit in order:
        upper = ((index >> bit) & 1) == 1
        received = exchanged(held, axis, 1 << bit)
        low = jnp.where(upper, received, held)
        high = jnp.where(upper, held, received)
        held = jnp.stack([low, high])
    done = len(order)
    natural = [done - 1 - order.index(bit) for bit in range(done - 1, -1, -1)]
    held = jnp.transpose(held, natural + list(range(done, held.ndim)))
    return held.reshape((-1,) + block.shape[1:])


def reduce_by_halves(chunks, axis, order):
    index = lax.axis_index(axis)
    done = len(order)
    held = chunks.reshape((2,) * done + chunks.shape[1:])
    held = jnp.transpose(held, [done - 1 - bit for bit in order] + list(range(done, held.ndim)))
    for bit in order:
        mine = (index >> bit) & 1
        kept = lax.dynamic_index_in_dim(held, mine, 0, keepdims=False)
        sent = lax.dynamic_index_in_dim(held, 1 - mine, 0, keepdims=False)
        received = exchanged(sent.astype(jnp.bfloat16), axis, 1 << bit)
        held = kept + received.astype(jnp.float32)
    return held.reshape((1,) + chunks.shape[1:])


def conv_forward(field, kernel):
    return lax.conv_general_dilated(
        field, kernel, (1, 1, 1), [(1, 1)] * 3,
        dimension_numbers=("NDHWC", "DHWIO", "NDHWC"),
        preferred_element_type=jnp.float32,
    )


def conv_transposed(slope, kernel):
    flipped = jnp.flip(kernel, (0, 1, 2))
    return lax.conv_general_dilated(
        slope, flipped, (1, 1, 1), [(1, 1)] * 3,
        dimension_numbers=("NDHWC", "DHWOI", "NDHWC"),
        preferred_element_type=jnp.float32,
    )


def conv_kernel_grad(field, slope):
    return lax.conv_general_dilated(
        field, slope, (1, 1, 1), [(1, 1)] * 3,
        dimension_numbers=("CDHWN", "IDHWO", "DHWNC"),
        preferred_element_type=jnp.float32,
    )


def position_term(anchor, pos_gain, size_x, size_y, size_z):
    phases = []
    for axis_num, axis_len in enumerate((size_x, size_y, size_z)):
        coords = anchor[axis_num] + STRIDE * jnp.arange(axis_len, dtype=jnp.int32)
        phase_val = (coords % WAVE).astype(jnp.float32)
        phases.append(jnp.sin(phase_val * (2.0 * math.pi / WAVE)))
    return (
        phases[0][:, None, None, None] * pos_gain[0]
        + phases[1][None, :, None, None] * pos_gain[1]
        + phases[2][None, None, :, None] * pos_gain[2]
    )


def local(acts, weights, pos_weight, anchors, top_grad):
    segments = lax.axis_size("segment")
    dp_count = lax.axis_size("dp")
    segment_index = lax.axis_index("segment")
    channels = weights.shape[2]
    bits = bit_count(dp_count)
    gather_order = list(range(bits - 2, 0, -1)) + [bits - 1, 0]
    gathered = gather_by_halves(weights[0][None], "dp", gather_order)
    kernel = gathered.reshape(3, 3, 3, channels, channels)
    fields = acts[0]
    micro_count, size_x, size_y, size_z = fields.shape[:4]
    cell_count = size_x * size_y * size_z
    pos_gain = pos_weight[0]
    position_all = jnp.stack(
        [position_term(anchors[m], pos_gain, size_x, size_y, size_z) for m in range(micro_count)]
    )
    pre_act = conv_forward(fields, kernel) + position_all
    sigmoid_h = jax.nn.sigmoid(pre_act)
    silu_slope = sigmoid_h * (1.0 + pre_act * (1.0 - sigmoid_h))

    is_top = segment_index == segments - 1
    incoming = jnp.zeros(top_grad.shape, jnp.bfloat16)
    grads_held = jnp.zeros(top_grad.shape, jnp.bfloat16)
    slope_held = jnp.zeros(top_grad.shape, jnp.bfloat16)
    for tick in range(segments):
        cotangent = jnp.where(is_top, top_grad, incoming).astype(jnp.float32)
        slope = (cotangent * silu_slope).astype(jnp.bfloat16)
        down_grad = (cotangent + conv_transposed(slope, kernel)).astype(jnp.bfloat16)
        mine = segment_index == segments - 1 - tick
        grads_held = jnp.where(mine, down_grad, grads_held)
        slope_held = jnp.where(mine, slope, slope_held)
        if tick + 1 < segments:
            incoming = passed_along(down_grad, "segment", -1)

    grad_term = conv_kernel_grad(fields, slope_held).reshape(dp_count, -1, channels)
    reduced = reduce_by_halves(grad_term, "dp", gather_order[::-1])
    scale_factor = 1.0 / math.sqrt(dp_count * micro_count * cell_count)
    return (grads_held[None], reduced * scale_factor)


def solution(mesh):
    return jax.shard_map(
        local,
        mesh=mesh,
        in_specs=(
            P("segment", "dp", None, None, None, None),
            P("segment", "dp", None),
            P("segment", None, None),
            P("dp", None),
            P("dp", None, None, None, None),
        ),
        out_specs=(P("segment", "dp", None, None, None, None), P("segment", "dp", None)),
        check_vma=False,
    )
```

```python
import math

import jax
import jax.numpy as jnp
from jax import lax
from jax.sharding import PartitionSpec as P

STRIDE = 2
WAVE = 64


def passed_along(array, axis, by):
    length = lax.axis_size(axis)
    pairs = [(i, i + by) for i in range(length) if 0 <= i + by < length]
    return lax.ppermute(array, axis, pairs)


def exchanged(array, axis, mask):
    length = lax.axis_size(axis)
    return lax.ppermute(array, axis, [(i, i ^ mask) for i in range(length)])


def bit_count(length):
    return length.bit_length() - 1


def group_value(index, group):
    width = len(group)
    return sum(((index >> bit) & 1) << (width - 1 - j) for j, bit in enumerate(group))


def group_mask(value, group):
    width = len(group)
    return sum(((value >> (width - 1 - j)) & 1) << bit for j, bit in enumerate(group))


def gather_by_groups(block, axis, groups):
    index = lax.axis_index(axis)
    held = block
    for group in groups:
        count = 1 << len(group)
        mine = group_value(index, group)
        pieces = [held] + [exchanged(held, axis, group_mask(m, group)) for m in range(1, count)]
        joined = jnp.zeros((count,) + held.shape, held.dtype)
        for m, piece in enumerate(pieces):
            joined = lax.dynamic_update_index_in_dim(joined, piece, mine ^ m, 0)
        held = joined
    order = [bit for group in groups[::-1] for bit in group]
    held = held.reshape((2,) * len(order) + block.shape)
    natural = [order.index(bit) for bit in range(len(order) - 1, -1, -1)]
    held = jnp.transpose(held, natural + list(range(len(order), held.ndim)))
    return held.reshape((-1,) + block.shape[1:])


def reduce_by_groups(chunks, axis, groups):
    index = lax.axis_index(axis)
    order = [bit for group in groups for bit in group]
    done = len(order)
    held = chunks.reshape((2,) * done + chunks.shape[1:])
    held = jnp.transpose(held, [done - 1 - bit for bit in order] + list(range(done, held.ndim)))
    held = held.reshape(tuple(1 << len(group) for group in groups) + chunks.shape[1:])
    for group in groups:
        count = 1 << len(group)
        mine = group_value(index, group)
        total = lax.dynamic_index_in_dim(held, mine, 0, keepdims=False)
        for m in range(1, count):
            sent = lax.dynamic_index_in_dim(held, mine ^ m, 0, keepdims=False)
            received = exchanged(sent.astype(jnp.bfloat16), axis, group_mask(m, group))
            total = total + received.astype(jnp.float32)
        held = total
    return held.reshape((1,) + chunks.shape[1:])


def conv_forward(field, kernel):
    return lax.conv_general_dilated(
        field, kernel, (1, 1, 1), [(1, 1)] * 3,
        dimension_numbers=("NDHWC", "DHWIO", "NDHWC"),
        preferred_element_type=jnp.float32,
    )


def conv_transposed(slope, kernel):
    flipped = jnp.flip(kernel, (0, 1, 2))
    return lax.conv_general_dilated(
        slope, flipped, (1, 1, 1), [(1, 1)] * 3,
        dimension_numbers=("NDHWC", "DHWOI", "NDHWC"),
        preferred_element_type=jnp.float32,
    )


def conv_kernel_grad(field, slope):
    return lax.conv_general_dilated(
        field, slope, (1, 1, 1), [(1, 1)] * 3,
        dimension_numbers=("CDHWN", "IDHWO", "DHWNC"),
        preferred_element_type=jnp.float32,
    )


def position_term(anchor, pos_gain, size_x, size_y, size_z):
    phases = []
    for axis_num, axis_len in enumerate((size_x, size_y, size_z)):
        coords = anchor[axis_num] + STRIDE * jnp.arange(axis_len, dtype=jnp.int32)
        phase_val = (coords % WAVE).astype(jnp.float32)
        phases.append(jnp.sin(phase_val * (2.0 * math.pi / WAVE)))
    return (
        phases[0][:, None, None, None] * pos_gain[0]
        + phases[1][None, :, None, None] * pos_gain[1]
        + phases[2][None, None, :, None] * pos_gain[2]
    )


def local(acts, weights, pos_weight, anchors, top_grad):
    segments = lax.axis_size("segment")
    dp_count = lax.axis_size("dp")
    segment_index = lax.axis_index("segment")
    channels = weights.shape[2]
    bits = bit_count(dp_count)
    gather_groups = [list(range(bits - 2, 1, -1)), [1, bits - 1, 0]]
    gathered = gather_by_groups(weights[0][None], "dp", gather_groups)
    kernel = gathered.reshape(3, 3, 3, channels, channels)
    fields = acts[0]
    micro_count, size_x, size_y, size_z = fields.shape[:4]
    cell_count = size_x * size_y * size_z
    pos_gain = pos_weight[0]
    position_all = jnp.stack(
        [position_term(anchors[m], pos_gain, size_x, size_y, size_z) for m in range(micro_count)]
    )
    pre_act = conv_forward(fields, kernel) + position_all
    sigmoid_h = jax.nn.sigmoid(pre_act)
    silu_slope = sigmoid_h * (1.0 + pre_act * (1.0 - sigmoid_h))

    is_top = segment_index == segments - 1
    incoming = jnp.zeros(top_grad.shape, jnp.bfloat16)
    grads_held = jnp.zeros(top_grad.shape, jnp.bfloat16)
    slope_held = jnp.zeros(top_grad.shape, jnp.bfloat16)
    for tick in range(segments):
        cotangent = jnp.where(is_top, top_grad, incoming).astype(jnp.float32)
        slope = (cotangent * silu_slope).astype(jnp.bfloat16)
        down_grad = (cotangent + conv_transposed(slope, kernel)).astype(jnp.bfloat16)
        mine = segment_index == segments - 1 - tick
        grads_held = jnp.where(mine, down_grad, grads_held)
        slope_held = jnp.where(mine, slope, slope_held)
        if tick + 1 < segments:
            incoming = passed_along(down_grad, "segment", -1)

    grad_term = conv_kernel_grad(fields, slope_held).reshape(dp_count, -1, channels)
    reduced = reduce_by_groups(grad_term, "dp", [group[::-1] for group in gather_groups[::-1]])
    scale_factor = 1.0 / math.sqrt(dp_count * micro_count * cell_count)
    return (grads_held[None], reduced * scale_factor)


def solution(mesh):
    return jax.shard_map(
        local,
        mesh=mesh,
        in_specs=(
            P("segment", "dp", None, None, None, None),
            P("segment", "dp", None),
            P("segment", None, None),
            P("dp", None),
            P("dp", None, None, None, None),
        ),
        out_specs=(P("segment", "dp", None, None, None, None), P("segment", "dp", None)),
        check_vma=False,
    )
```

```python
import math

import jax
import jax.numpy as jnp
from jax import lax
from jax.sharding import PartitionSpec as P

STRIDE = 2
WAVE = 64


def passed_along(array, axis, by):
    length = lax.axis_size(axis)
    pairs = [(i, i + by) for i in range(length) if 0 <= i + by < length]
    return lax.ppermute(array, axis, pairs)


def exchanged(array, axis, mask):
    length = lax.axis_size(axis)
    return lax.ppermute(array, axis, [(i, i ^ mask) for i in range(length)])


def bit_count(length):
    return length.bit_length() - 1


def gather_by_halves(block, axis, order):
    index = lax.axis_index(axis)
    held = block
    for bit in order:
        upper = ((index >> bit) & 1) == 1
        received = exchanged(held, axis, 1 << bit)
        low = jnp.where(upper, received, held)
        high = jnp.where(upper, held, received)
        held = jnp.stack([low, high])
    done = len(order)
    natural = [done - 1 - order.index(bit) for bit in range(done - 1, -1, -1)]
    held = jnp.transpose(held, natural + list(range(done, held.ndim)))
    return held.reshape((-1,) + block.shape[1:])


def reduce_by_halves(chunks, axis, order):
    index = lax.axis_index(axis)
    done = len(order)
    held = chunks.reshape((2,) * done + chunks.shape[1:])
    held = jnp.transpose(held, [done - 1 - bit for bit in order] + list(range(done, held.ndim)))
    for bit in order:
        mine = (index >> bit) & 1
        kept = lax.dynamic_index_in_dim(held, mine, 0, keepdims=False)
        sent = lax.dynamic_index_in_dim(held, 1 - mine, 0, keepdims=False)
        received = exchanged(sent.astype(jnp.bfloat16), axis, 1 << bit)
        held = kept + received.astype(jnp.float32)
    return held.reshape((1,) + chunks.shape[1:])


def conv_forward(field, kernel):
    return lax.conv_general_dilated(
        field, kernel, (1, 1, 1), [(1, 1)] * 3,
        dimension_numbers=("NDHWC", "DHWIO", "NDHWC"),
        preferred_element_type=jnp.float32,
    )


def conv_transposed(slope, kernel):
    flipped = jnp.flip(kernel, (0, 1, 2))
    return lax.conv_general_dilated(
        slope, flipped, (1, 1, 1), [(1, 1)] * 3,
        dimension_numbers=("NDHWC", "DHWOI", "NDHWC"),
        preferred_element_type=jnp.float32,
    )


def conv_kernel_grad(field, slope):
    return lax.conv_general_dilated(
        field, slope, (1, 1, 1), [(1, 1)] * 3,
        dimension_numbers=("CDHWN", "IDHWO", "DHWNC"),
        preferred_element_type=jnp.float32,
    )


def position_term(anchor, pos_gain, size_x, size_y, size_z):
    phases = []
    for axis_num, axis_len in enumerate((size_x, size_y, size_z)):
        coords = anchor[axis_num] + STRIDE * jnp.arange(axis_len, dtype=jnp.int32)
        phase_val = (coords % WAVE).astype(jnp.float32)
        phases.append(jnp.sin(phase_val * (2.0 * math.pi / WAVE)))
    return (
        phases[0][:, None, None, None] * pos_gain[0]
        + phases[1][None, :, None, None] * pos_gain[1]
        + phases[2][None, None, :, None] * pos_gain[2]
    )


def local(acts, weights, pos_weight, anchors, top_grad):
    segments = lax.axis_size("segment")
    dp_count = lax.axis_size("dp")
    segment_index = lax.axis_index("segment")
    channels = weights.shape[2]
    bits = bit_count(dp_count)
    gather_order = list(range(bits - 2, 0, -1)) + [bits - 1, 0]
    gathered = gather_by_halves(weights[0][None], "dp", gather_order)
    kernel = gathered.reshape(3, 3, 3, channels, channels)
    fields = acts[0]
    micro_count, size_x, size_y, size_z = fields.shape[:4]
    cell_count = size_x * size_y * size_z
    pos_gain = pos_weight[0]
    position_all = jnp.stack(
        [position_term(anchors[m], pos_gain, size_x, size_y, size_z) for m in range(micro_count)]
    )
    pre_act = conv_forward(fields, kernel) + position_all
    sigmoid_h = jax.nn.sigmoid(pre_act)
    silu_slope = sigmoid_h * (1.0 + pre_act * (1.0 - sigmoid_h))

    is_top = segment_index == segments - 1
    incoming = jnp.zeros(top_grad.shape, jnp.bfloat16)
    grads_held = jnp.zeros(top_grad.shape, jnp.bfloat16)
    slope_held = jnp.zeros(top_grad.shape, jnp.bfloat16)
    for tick in range(segments):
        cotangent = jnp.where(is_top, top_grad, incoming).astype(jnp.float32)
        slope = (cotangent * silu_slope).astype(jnp.bfloat16)
        down_grad = (cotangent + conv_transposed(slope, kernel)).astype(jnp.bfloat16)
        mine = segment_index == segments - 1 - tick
        grads_held = jnp.where(mine, down_grad, grads_held)
        slope_held = jnp.where(mine, slope, slope_held)
        if tick + 1 < segments:
            sender = segments - 1 - tick
            incoming = lax.ppermute(down_grad, "segment", [(sender, sender - 1)])

    grad_term = conv_kernel_grad(fields, slope_held).reshape(dp_count, -1, channels)
    reduced = reduce_by_halves(grad_term, "dp", gather_order[::-1])
    scale_factor = 1.0 / math.sqrt(dp_count * micro_count * cell_count)
    return (grads_held[None], reduced * scale_factor)


def solution(mesh):
    return jax.shard_map(
        local,
        mesh=mesh,
        in_specs=(
            P("segment", "dp", None, None, None, None),
            P("segment", "dp", None),
            P("segment", None, None),
            P("dp", None),
            P("dp", None, None, None, None),
        ),
        out_specs=(P("segment", "dp", None, None, None, None), P("segment", "dp", None)),
        check_vma=False,
    )
```

```python
import math

import jax
import jax.numpy as jnp
from jax import lax
from jax.sharding import PartitionSpec as P

DP = ("y", "z", "core")
STRIDE = 2
WAVE = 64


def passed_along(array, axis, by):
    length = lax.axis_size(axis)
    pairs = [(i, i + by) for i in range(length) if 0 <= i + by < length]
    return lax.ppermute(array, axis, pairs)


def exchanged(array, axis, mask):
    length = lax.axis_size(axis)
    return lax.ppermute(array, axis, [(i, i ^ mask) for i in range(length)])


def bit_count(length):
    return length.bit_length() - 1


def gather_by_halves(block, axis, order):
    index = lax.axis_index(axis)
    held = block
    for bit in order:
        upper = ((index >> bit) & 1) == 1
        received = exchanged(held, axis, 1 << bit)
        low = jnp.where(upper, received, held)
        high = jnp.where(upper, held, received)
        held = jnp.stack([low, high])
    done = len(order)
    natural = [done - 1 - order.index(bit) for bit in range(done - 1, -1, -1)]
    held = jnp.transpose(held, natural + list(range(done, held.ndim)))
    return held.reshape((-1,) + block.shape[1:])


def reduce_by_halves(chunks, axis, order, ring_axis):
    index = lax.axis_index(axis)
    done = bit_count(chunks.shape[0])
    rest = [bit for bit in range(done - 1, -1, -1) if bit not in order]
    held = chunks.reshape((2,) * done + chunks.shape[1:])
    held = jnp.transpose(held, [done - 1 - bit for bit in order + rest] + list(range(done, held.ndim)))
    for bit in order:
        mine = (index >> bit) & 1
        kept = lax.dynamic_index_in_dim(held, mine, 0, keepdims=False)
        sent = lax.dynamic_index_in_dim(held, 1 - mine, 0, keepdims=False)
        received = exchanged(sent.astype(jnp.bfloat16), axis, 1 << bit)
        held = kept + received.astype(jnp.float32)
    held = held.reshape((-1,) + chunks.shape[1:]).astype(jnp.bfloat16)
    received = lax.all_to_all(held, ring_axis, 0, 0, tiled=True)
    return jnp.sum(received.astype(jnp.float32), axis=0, keepdims=True)


def conv_forward(field, kernel):
    return lax.conv_general_dilated(
        field, kernel, (1, 1, 1), [(1, 1)] * 3,
        dimension_numbers=("NDHWC", "DHWIO", "NDHWC"),
        preferred_element_type=jnp.float32,
    )


def conv_transposed(slope, kernel):
    flipped = jnp.flip(kernel, (0, 1, 2))
    return lax.conv_general_dilated(
        slope, flipped, (1, 1, 1), [(1, 1)] * 3,
        dimension_numbers=("NDHWC", "DHWOI", "NDHWC"),
        preferred_element_type=jnp.float32,
    )


def conv_kernel_grad(field, slope):
    return lax.conv_general_dilated(
        field, slope, (1, 1, 1), [(1, 1)] * 3,
        dimension_numbers=("CDHWN", "IDHWO", "DHWNC"),
        preferred_element_type=jnp.float32,
    )


def position_term(anchor, pos_gain, size_x, size_y, size_z):
    phases = []
    for axis_num, axis_len in enumerate((size_x, size_y, size_z)):
        coords = anchor[axis_num] + STRIDE * jnp.arange(axis_len, dtype=jnp.int32)
        phase_val = (coords % WAVE).astype(jnp.float32)
        phases.append(jnp.sin(phase_val * (2.0 * math.pi / WAVE)))
    return (
        phases[0][:, None, None, None] * pos_gain[0]
        + phases[1][None, :, None, None] * pos_gain[1]
        + phases[2][None, None, :, None] * pos_gain[2]
    )


def local(acts, weights, pos_weight, anchors, top_grad):
    segments = lax.axis_size("segment")
    dp_count = lax.axis_size(DP)
    segment_index = lax.axis_index("segment")
    channels = weights.shape[2]
    bits = bit_count(dp_count)
    gather_order = list(range(bits - 2, 0, -1)) + [bits - 1, 0]
    gathered = gather_by_halves(weights[0][None], DP, gather_order)
    kernel = gathered.reshape(3, 3, 3, channels, channels)
    fields = acts[0]
    micro_count, size_x, size_y, size_z = fields.shape[:4]
    cell_count = size_x * size_y * size_z
    pos_gain = pos_weight[0]
    position_all = jnp.stack(
        [position_term(anchors[m], pos_gain, size_x, size_y, size_z) for m in range(micro_count)]
    )
    pre_act = conv_forward(fields, kernel) + position_all
    sigmoid_h = jax.nn.sigmoid(pre_act)
    silu_slope = sigmoid_h * (1.0 + pre_act * (1.0 - sigmoid_h))

    is_top = segment_index == segments - 1
    incoming = jnp.zeros(top_grad.shape, jnp.bfloat16)
    grads_held = jnp.zeros(top_grad.shape, jnp.bfloat16)
    slope_held = jnp.zeros(top_grad.shape, jnp.bfloat16)
    for tick in range(segments):
        cotangent = jnp.where(is_top, top_grad, incoming).astype(jnp.float32)
        slope = (cotangent * silu_slope).astype(jnp.bfloat16)
        down_grad = (cotangent + conv_transposed(slope, kernel)).astype(jnp.bfloat16)
        mine = segment_index == segments - 1 - tick
        grads_held = jnp.where(mine, down_grad, grads_held)
        slope_held = jnp.where(mine, slope, slope_held)
        if tick + 1 < segments:
            sender = segments - 1 - tick
            incoming = lax.ppermute(down_grad, "segment", [(sender, sender - 1)])

    scale_factor = 1.0 / math.sqrt(dp_count * micro_count * cell_count)
    grad_term = conv_kernel_grad(fields, slope_held) * scale_factor
    grad_term = grad_term.reshape(dp_count, -1, channels)
    reduced = reduce_by_halves(grad_term, DP, [0, bits - 1], "z")
    return (grads_held[None], reduced)


def solution(mesh):
    segments, dp_count = mesh.devices.shape
    fine = jax.sharding.Mesh(
        mesh.devices.reshape(segments, 2, dp_count // 4, 2), ("segment",) + DP
    )
    return jax.shard_map(
        local,
        mesh=fine,
        in_specs=(
            P("segment", DP, None, None, None, None),
            P("segment", DP, None),
            P("segment", None, None),
            P(DP, None),
            P(DP, None, None, None, None),
        ),
        out_specs=(P("segment", DP, None, None, None, None), P("segment", DP, None)),
        check_vma=False,
    )
```

```python
import math

import jax
import jax.numpy as jnp
from jax import lax
from jax.sharding import PartitionSpec as P

DP = ("y", "z", "core")
STRIDE = 2
WAVE = 64


def passed_along(array, axis, by):
    length = lax.axis_size(axis)
    pairs = [(i, i + by) for i in range(length) if 0 <= i + by < length]
    return lax.ppermute(array, axis, pairs)


def exchanged(array, axis, mask):
    length = lax.axis_size(axis)
    return lax.ppermute(array, axis, [(i, i ^ mask) for i in range(length)])


def bit_count(length):
    return length.bit_length() - 1


def gather_by_halves(block, axis, order, ring_axis):
    index = lax.axis_index(axis)
    ring = lax.axis_size(ring_axis)
    held = lax.all_to_all(jnp.broadcast_to(block, (ring,) + block.shape), ring_axis, 0, 0, tiled=True)
    for bit in order:
        upper = ((index >> bit) & 1) == 1
        received = exchanged(held, axis, 1 << bit)
        low = jnp.where(upper, received, held)
        high = jnp.where(upper, held, received)
        held = jnp.stack([low, high])
    held = jnp.moveaxis(held, 0, len(order))
    return held.reshape((-1,) + block.shape[1:])


def reduce_by_halves(chunks, axis, order, ring_axis):
    index = lax.axis_index(axis)
    done = bit_count(chunks.shape[0])
    rest = [bit for bit in range(done - 1, -1, -1) if bit not in order]
    held = chunks.reshape((2,) * done + chunks.shape[1:])
    held = jnp.transpose(held, [done - 1 - bit for bit in order + rest] + list(range(done, held.ndim)))
    for bit in order:
        mine = (index >> bit) & 1
        kept = lax.dynamic_index_in_dim(held, mine, 0, keepdims=False)
        sent = lax.dynamic_index_in_dim(held, 1 - mine, 0, keepdims=False)
        received = exchanged(sent.astype(jnp.bfloat16), axis, 1 << bit)
        held = kept + received.astype(jnp.float32)
    held = held.reshape((-1,) + chunks.shape[1:]).astype(jnp.bfloat16)
    received = lax.all_to_all(held, ring_axis, 0, 0, tiled=True)
    return jnp.sum(received.astype(jnp.float32), axis=0, keepdims=True)


def conv_forward(field, kernel):
    return lax.conv_general_dilated(
        field, kernel, (1, 1, 1), [(1, 1)] * 3,
        dimension_numbers=("NDHWC", "DHWIO", "NDHWC"),
        preferred_element_type=jnp.float32,
    )


def conv_transposed(slope, kernel):
    flipped = jnp.flip(kernel, (0, 1, 2))
    return lax.conv_general_dilated(
        slope, flipped, (1, 1, 1), [(1, 1)] * 3,
        dimension_numbers=("NDHWC", "DHWOI", "NDHWC"),
        preferred_element_type=jnp.float32,
    )


def conv_kernel_grad(field, slope):
    return lax.conv_general_dilated(
        field, slope, (1, 1, 1), [(1, 1)] * 3,
        dimension_numbers=("CDHWN", "IDHWO", "DHWNC"),
        preferred_element_type=jnp.float32,
    )


def position_terms(anchors, pos_gain, size_x, size_y, size_z):
    longest = max(size_x, size_y, size_z)
    coords = anchors[:, :, None] + STRIDE * jnp.arange(longest, dtype=jnp.int32)
    phases = jnp.sin((coords % WAVE).astype(jnp.float32) * (2.0 * math.pi / WAVE))
    return (
        phases[:, 0, :size_x, None, None, None] * pos_gain[0]
        + phases[:, 1, None, :size_y, None, None] * pos_gain[1]
        + phases[:, 2, None, None, :size_z, None] * pos_gain[2]
    )


def local(acts, weights, pos_weight, anchors, top_grad):
    segments = lax.axis_size("segment")
    dp_count = lax.axis_size(DP)
    segment_index = lax.axis_index("segment")
    channels = weights.shape[2]
    bits = bit_count(dp_count)
    gathered = gather_by_halves(weights[0], DP, [bits - 1, 0], "z")
    kernel = gathered.reshape(3, 3, 3, channels, channels)
    fields = acts[0]
    micro_count, size_x, size_y, size_z = fields.shape[:4]
    cell_count = size_x * size_y * size_z
    pos_gain = pos_weight[0]
    position_all = position_terms(anchors, pos_gain, size_x, size_y, size_z)
    pre_act = conv_forward(fields, kernel) + position_all
    sigmoid_h = jax.nn.sigmoid(pre_act)
    silu_slope = sigmoid_h * (1.0 + pre_act * (1.0 - sigmoid_h))

    is_top = segment_index == segments - 1
    incoming = jnp.zeros(top_grad.shape, jnp.bfloat16)
    grads_held = jnp.zeros(top_grad.shape, jnp.bfloat16)
    slope_held = jnp.zeros(top_grad.shape, jnp.bfloat16)
    for tick in range(segments):
        cotangent = jnp.where(is_top, top_grad, incoming).astype(jnp.float32)
        slope = (cotangent * silu_slope).astype(jnp.bfloat16)
        down_grad = (cotangent + conv_transposed(slope, kernel)).astype(jnp.bfloat16)
        mine = segment_index == segments - 1 - tick
        grads_held = jnp.where(mine, down_grad, grads_held)
        slope_held = jnp.where(mine, slope, slope_held)
        if tick + 1 < segments:
            sender = segments - 1 - tick
            incoming = lax.ppermute(down_grad, "segment", [(sender, sender - 1)])

    scale_factor = 1.0 / math.sqrt(dp_count * micro_count * cell_count)
    grad_term = conv_kernel_grad(fields, slope_held) * scale_factor
    grad_term = grad_term.reshape(dp_count, -1, channels)
    reduced = reduce_by_halves(grad_term, DP, [0, bits - 1], "z")
    return (grads_held[None], reduced)


def solution(mesh):
    segments, dp_count = mesh.devices.shape
    fine = jax.sharding.Mesh(
        mesh.devices.reshape(segments, 2, dp_count // 4, 2), ("segment",) + DP
    )
    return jax.shard_map(
        local,
        mesh=fine,
        in_specs=(
            P("segment", DP, None, None, None, None),
            P("segment", DP, None),
            P("segment", None, None),
            P(DP, None),
            P(DP, None, None, None, None),
        ),
        out_specs=(P("segment", DP, None, None, None, None), P("segment", DP, None)),
        check_vma=False,
    )
```

```python
import math

import jax
import jax.numpy as jnp
from jax import lax
from jax.sharding import PartitionSpec as P

DP = ("y", "z", "core")
STRIDE = 2
WAVE = 64


def passed_along(array, axis, by):
    length = lax.axis_size(axis)
    pairs = [(i, i + by) for i in range(length) if 0 <= i + by < length]
    return lax.ppermute(array, axis, pairs)


def exchanged(array, axis, mask):
    length = lax.axis_size(axis)
    return lax.ppermute(array, axis, [(i, i ^ mask) for i in range(length)])


def bit_count(length):
    return length.bit_length() - 1


def gather_by_halves(block, axis, order, ring_axis):
    index = lax.axis_index(axis)
    ring = lax.axis_size(ring_axis)
    held = lax.all_to_all(jnp.broadcast_to(block, (ring,) + block.shape), ring_axis, 0, 0, tiled=True)
    for bit in order:
        upper = ((index >> bit) & 1) == 1
        received = exchanged(held, axis, 1 << bit)
        low = jnp.where(upper, received, held)
        high = jnp.where(upper, held, received)
        held = jnp.stack([low, high])
    held = jnp.moveaxis(held, 0, len(order))
    return held.reshape((-1,) + block.shape[1:])


def reduce_by_halves(chunks, axis, order, ring_axis):
    index = lax.axis_index(axis)
    done = bit_count(chunks.shape[0])
    rest = [bit for bit in range(done - 1, -1, -1) if bit not in order]
    held = chunks.reshape((2,) * done + chunks.shape[1:])
    held = jnp.transpose(held, [done - 1 - bit for bit in order + rest] + list(range(done, held.ndim)))
    for bit in order:
        mine = (index >> bit) & 1
        kept = lax.dynamic_index_in_dim(held, mine, 0, keepdims=False)
        sent = lax.dynamic_index_in_dim(held, 1 - mine, 0, keepdims=False)
        received = exchanged(sent.astype(jnp.bfloat16), axis, 1 << bit)
        held = kept + received.astype(jnp.float32)
    held = held.reshape((-1,) + chunks.shape[1:]).astype(jnp.bfloat16)
    received = lax.all_to_all(held, ring_axis, 0, 0, tiled=True)
    return jnp.sum(received.astype(jnp.float32), axis=0, keepdims=True)


def conv_forward(field, kernel):
    return lax.conv_general_dilated(
        field, kernel, (1, 1, 1), [(1, 1)] * 3,
        dimension_numbers=("NDHWC", "DHWIO", "NDHWC"),
        preferred_element_type=jnp.float32,
    )


def conv_transposed(slope, kernel):
    flipped = jnp.flip(kernel, (0, 1, 2))
    return lax.conv_general_dilated(
        slope, flipped, (1, 1, 1), [(1, 1)] * 3,
        dimension_numbers=("NDHWC", "DHWOI", "NDHWC"),
        preferred_element_type=jnp.float32,
    )


def conv_kernel_grad(field, slope):
    return lax.conv_general_dilated(
        field, slope, (1, 1, 1), [(1, 1)] * 3,
        dimension_numbers=("CDHWN", "IDHWO", "DHWNC"),
        preferred_element_type=jnp.float32,
    )


def position_terms(anchors, pos_gain, size_x, size_y, size_z):
    longest = max(size_x, size_y, size_z)
    coords = anchors[:, :, None] + STRIDE * jnp.arange(longest, dtype=jnp.int32)
    phases = jnp.sin((coords % WAVE).astype(jnp.float32) * (2.0 * math.pi / WAVE))
    return (
        phases[:, 0, :size_x, None, None, None] * pos_gain[0]
        + phases[:, 1, None, :size_y, None, None] * pos_gain[1]
        + phases[:, 2, None, None, :size_z, None] * pos_gain[2]
    )


def silu_slopes(field, kernel, anchors, pos_gain):
    size_x, size_y, size_z = field.shape[1:4]
    pre_act = conv_forward(field, kernel) + position_terms(anchors, pos_gain, size_x, size_y, size_z)
    sigmoid_h = jax.nn.sigmoid(pre_act)
    return sigmoid_h * (1.0 + pre_act * (1.0 - sigmoid_h))


def section_step(cotangent, silu_slope, kernel):
    slope = (cotangent * silu_slope).astype(jnp.bfloat16)
    down_grad = (cotangent + conv_transposed(slope, kernel)).astype(jnp.bfloat16)
    return slope, down_grad


def split_exact(values):
    high = values.astype(jnp.bfloat16)
    rest = values - high.astype(jnp.float32)
    middle = rest.astype(jnp.bfloat16)
    low = (rest - middle.astype(jnp.float32)).astype(jnp.bfloat16)
    return [high, middle, low]


def local(acts, weights, pos_weight, anchors, top_grad):
    segments = lax.axis_size("segment")
    dp_count = lax.axis_size(DP)
    segment_index = lax.axis_index("segment")
    channels = weights.shape[2]
    rows = weights.shape[1]
    bits = bit_count(dp_count)
    fields = acts[0]
    micro_count, size_x, size_y, size_z = fields.shape[:4]
    cell_count = size_x * size_y * size_z
    gain_rows = pos_weight.shape[1]

    packed = jnp.concatenate(
        [weights[0], fields.reshape(-1, channels)] + split_exact(pos_weight[0]), axis=0
    )
    upper = lax.ppermute(packed, "segment", [(i + 1, i) for i in range(segments - 1)])
    weights_up = upper[:rows]
    fields_up = upper[rows : rows + micro_count * cell_count].reshape(fields.shape)
    gain_parts = upper[rows + micro_count * cell_count :].astype(jnp.float32)
    gain_up = (
        gain_parts[:gain_rows] + gain_parts[gain_rows : 2 * gain_rows]
    ) + gain_parts[2 * gain_rows :]

    both = jnp.concatenate([weights[0], weights_up], axis=1)
    gathered = gather_by_halves(both, DP, [bits - 1, 0], "z")
    kernel = gathered[:, :channels].reshape(3, 3, 3, channels, channels)
    kernel_up = gathered[:, channels:].reshape(3, 3, 3, channels, channels)
    silu_own = silu_slopes(fields, kernel, anchors, pos_weight[0])
    silu_up = silu_slopes(fields_up, kernel_up, anchors, gain_up)

    received = jnp.zeros(top_grad.shape, jnp.bfloat16)
    grads_held = jnp.zeros(top_grad.shape, jnp.bfloat16)
    slope_held = jnp.zeros(top_grad.shape, jnp.bfloat16)
    stages = (segments + 1) // 2
    for stage in range(stages):
        high = segments - 1 - 2 * stage
        cotangent = jnp.where(segment_index == segments - 2, top_grad, received)
        _, above = section_step(cotangent.astype(jnp.float32), silu_up, kernel_up)
        cotangent = jnp.where(segment_index == segments - 1, top_grad, above)
        slope, down_grad = section_step(cotangent.astype(jnp.float32), silu_own, kernel)
        mine = (segment_index == high) | (segment_index == high - 1)
        grads_held = jnp.where(mine, down_grad, grads_held)
        slope_held = jnp.where(mine, slope, slope_held)
        pairs = [(source, source - 2) for source in (high, high - 1) if source - 2 >= 0]
        if pairs:
            received = lax.ppermute(down_grad, "segment", pairs)

    scale_factor = 1.0 / math.sqrt(dp_count * micro_count * cell_count)
    grad_term = conv_kernel_grad(fields, slope_held) * scale_factor
    grad_term = grad_term.reshape(dp_count, -1, channels)
    reduced = reduce_by_halves(grad_term, DP, [0, bits - 1], "z")
    return (grads_held[None], reduced)


def solution(mesh):
    segments, dp_count = mesh.devices.shape
    fine = jax.sharding.Mesh(
        mesh.devices.reshape(segments, 2, dp_count // 4, 2), ("segment",) + DP
    )
    return jax.shard_map(
        local,
        mesh=fine,
        in_specs=(
            P("segment", DP, None, None, None, None),
            P("segment", DP, None),
            P("segment", None, None),
            P(DP, None),
            P(DP, None, None, None, None),
        ),
        out_specs=(P("segment", DP, None, None, None, None), P("segment", DP, None)),
        check_vma=False,
    )
```

```python
import math

import jax
import jax.numpy as jnp
from jax import lax
from jax.sharding import PartitionSpec as P

DP = ("y", "z", "core")
STRIDE = 2
WAVE = 64


def passed_along(array, axis, by):
    length = lax.axis_size(axis)
    pairs = [(i, i + by) for i in range(length) if 0 <= i + by < length]
    return lax.ppermute(array, axis, pairs)


def exchanged(array, axis, mask):
    length = lax.axis_size(axis)
    return lax.ppermute(array, axis, [(i, i ^ mask) for i in range(length)])


def bit_count(length):
    return length.bit_length() - 1


def gather_by_halves(block, axis, order, ring_axis):
    index = lax.axis_index(axis)
    ring = lax.axis_size(ring_axis)
    held = lax.all_to_all(jnp.broadcast_to(block, (ring,) + block.shape), ring_axis, 0, 0, tiled=True)
    for bit in order:
        upper = ((index >> bit) & 1) == 1
        received = exchanged(held, axis, 1 << bit)
        low = jnp.where(upper, received, held)
        high = jnp.where(upper, held, received)
        held = jnp.stack([low, high])
    held = jnp.moveaxis(held, 0, len(order))
    return held.reshape((-1,) + block.shape[1:])


def reduce_by_halves(chunks, axis, ring_axis):
    index = lax.axis_index(axis)
    ring = lax.axis_size(ring_axis)
    held = chunks.reshape((2, ring, 2) + chunks.shape[1:])
    mine = index & 1
    kept = lax.dynamic_index_in_dim(held, mine, 2, keepdims=False)
    sent = lax.dynamic_index_in_dim(held, 1 - mine, 2, keepdims=False)
    received = exchanged(sent.astype(jnp.bfloat16), axis, 1)
    held = kept + received.astype(jnp.float32)
    top = bit_count(lax.axis_size(axis)) - 1
    mine = (index >> top) & 1
    kept = lax.dynamic_index_in_dim(held, mine, 0, keepdims=False)
    sent = lax.dynamic_index_in_dim(held, 1 - mine, 0, keepdims=False)
    received = exchanged(sent.astype(jnp.bfloat16), axis, 1 << top)
    held = (kept + received.astype(jnp.float32)).astype(jnp.bfloat16)
    received = lax.all_to_all(held, ring_axis, 0, 0, tiled=True)
    return jnp.sum(received.astype(jnp.float32), axis=0, keepdims=True)


def conv_forward(field, kernel):
    return lax.conv_general_dilated(
        field, kernel, (1, 1, 1), [(1, 1)] * 3,
        dimension_numbers=("NDHWC", "DHWIO", "NDHWC"),
        preferred_element_type=jnp.float32,
    )


def conv_transposed(slope, kernel):
    flipped = jnp.flip(kernel, (0, 1, 2))
    return lax.conv_general_dilated(
        slope, flipped, (1, 1, 1), [(1, 1)] * 3,
        dimension_numbers=("NDHWC", "DHWOI", "NDHWC"),
        preferred_element_type=jnp.float32,
    )


def conv_kernel_grad(field, slope):
    return lax.conv_general_dilated(
        field, slope, (1, 1, 1), [(1, 1)] * 3,
        dimension_numbers=("CDHWN", "IDHWO", "DHWNC"),
        preferred_element_type=jnp.float32,
    )


def position_terms(anchors, pos_gain, size_x, size_y, size_z):
    longest = max(size_x, size_y, size_z)
    coords = anchors[:, :, None] + STRIDE * jnp.arange(longest, dtype=jnp.int32)
    phases = jnp.sin((coords % WAVE).astype(jnp.float32) * (2.0 * math.pi / WAVE))
    return (
        phases[:, 0, :size_x, None, None, None] * pos_gain[0]
        + phases[:, 1, None, :size_y, None, None] * pos_gain[1]
        + phases[:, 2, None, None, :size_z, None] * pos_gain[2]
    )


def local(acts, weights, pos_weight, anchors, top_grad):
    segments = lax.axis_size("segment")
    dp_count = lax.axis_size(DP)
    segment_index = lax.axis_index("segment")
    channels = weights.shape[2]
    bits = bit_count(dp_count)
    gathered = gather_by_halves(weights[0], DP, [bits - 1, 0], "z")
    kernel = gathered.reshape(3, 3, 3, channels, channels)
    fields = acts[0]
    micro_count, size_x, size_y, size_z = fields.shape[:4]
    cell_count = size_x * size_y * size_z
    pos_gain = pos_weight[0]
    position_all = position_terms(anchors, pos_gain, size_x, size_y, size_z)
    pre_act = conv_forward(fields, kernel) + position_all
    sigmoid_h = jax.nn.sigmoid(pre_act)
    silu_slope = sigmoid_h * (1.0 + pre_act * (1.0 - sigmoid_h))

    is_top = segment_index == segments - 1
    incoming = jnp.zeros(top_grad.shape, jnp.bfloat16)
    grads_held = jnp.zeros(top_grad.shape, jnp.bfloat16)
    slope_held = jnp.zeros(top_grad.shape, jnp.bfloat16)
    for tick in range(segments):
        cotangent = jnp.where(is_top, top_grad, incoming).astype(jnp.float32)
        slope = (cotangent * silu_slope).astype(jnp.bfloat16)
        down_grad = (cotangent + conv_transposed(slope, kernel)).astype(jnp.bfloat16)
        mine = segment_index == segments - 1 - tick
        grads_held = jnp.where(mine, down_grad, grads_held)
        slope_held = jnp.where(mine, slope, slope_held)
        if tick + 1 < segments:
            sender = segments - 1 - tick
            incoming = lax.ppermute(down_grad, "segment", [(sender, sender - 1)])

    scale_factor = 1.0 / math.sqrt(dp_count * micro_count * cell_count)
    grad_term = conv_kernel_grad(fields, slope_held) * scale_factor
    grad_term = grad_term.reshape(dp_count, -1, channels)
    reduced = reduce_by_halves(grad_term, DP, "z")
    return (grads_held[None], reduced)


def solution(mesh):
    segments, dp_count = mesh.devices.shape
    fine = jax.sharding.Mesh(
        mesh.devices.reshape(segments, 2, dp_count // 4, 2), ("segment",) + DP
    )
    return jax.shard_map(
        local,
        mesh=fine,
        in_specs=(
            P("segment", DP, None, None, None, None),
            P("segment", DP, None),
            P("segment", None, None),
            P(DP, None),
            P(DP, None, None, None, None),
        ),
        out_specs=(P("segment", DP, None, None, None, None), P("segment", DP, None)),
        check_vma=False,
    )
```

```python
import math

import jax
import jax.numpy as jnp
from jax import lax
from jax.sharding import PartitionSpec as P

DP = ("y", "z", "core")
STRIDE = 2
WAVE = 64


def passed_along(array, axis, by):
    length = lax.axis_size(axis)
    pairs = [(i, i + by) for i in range(length) if 0 <= i + by < length]
    return lax.ppermute(array, axis, pairs)


def exchanged(array, axis, mask):
    length = lax.axis_size(axis)
    return lax.ppermute(array, axis, [(i, i ^ mask) for i in range(length)])


def bit_count(length):
    return length.bit_length() - 1


def gather_by_halves(block, axis, order, ring_axis):
    index = lax.axis_index(axis)
    ring = lax.axis_size(ring_axis)
    held = lax.all_to_all(jnp.broadcast_to(block, (ring,) + block.shape), ring_axis, 0, 0, tiled=True)
    for bit in order:
        upper = ((index >> bit) & 1) == 1
        received = exchanged(held, axis, 1 << bit)
        low = jnp.where(upper, received, held)
        high = jnp.where(upper, held, received)
        held = jnp.stack([low, high])
    held = jnp.moveaxis(held, 0, len(order))
    return held.reshape((-1,) + block.shape[1:])


def reduce_by_halves(chunks, axis, order, ring_axis):
    index = lax.axis_index(axis)
    done = bit_count(chunks.shape[0])
    rest = [bit for bit in range(done - 1, -1, -1) if bit not in order]
    held = chunks.reshape((2,) * done + chunks.shape[1:])
    held = jnp.transpose(held, [done - 1 - bit for bit in order + rest] + list(range(done, held.ndim)))
    for bit in order:
        mine = (index >> bit) & 1
        kept = lax.dynamic_index_in_dim(held, mine, 0, keepdims=False)
        sent = lax.dynamic_index_in_dim(held, 1 - mine, 0, keepdims=False)
        received = exchanged(sent.astype(jnp.bfloat16), axis, 1 << bit)
        held = kept + received.astype(jnp.float32)
    held = held.reshape((-1,) + chunks.shape[1:]).astype(jnp.bfloat16)
    received = lax.all_to_all(held, ring_axis, 0, 0, tiled=True)
    return jnp.sum(received.astype(jnp.float32), axis=0, keepdims=True)


def conv_forward(field, kernel):
    return lax.conv_general_dilated(
        field, kernel, (1, 1, 1), [(1, 1)] * 3,
        dimension_numbers=("NDHWC", "DHWIO", "NDHWC"),
        preferred_element_type=jnp.float32,
    )


def conv_transposed(slope, kernel):
    flipped = jnp.flip(kernel, (0, 1, 2))
    return lax.conv_general_dilated(
        slope, flipped, (1, 1, 1), [(1, 1)] * 3,
        dimension_numbers=("NDHWC", "DHWOI", "NDHWC"),
        preferred_element_type=jnp.float32,
    )


def conv_kernel_grad(field, slope):
    return lax.conv_general_dilated(
        field, slope, (1, 1, 1), [(1, 1)] * 3,
        dimension_numbers=("CDHWN", "IDHWO", "DHWNC"),
        preferred_element_type=jnp.float32,
    )


def position_terms(anchors, pos_gain, size_x, size_y, size_z):
    longest = max(size_x, size_y, size_z)
    coords = anchors[:, :, None] + STRIDE * jnp.arange(longest, dtype=jnp.int32)
    phases = jnp.sin((coords % WAVE).astype(jnp.float32) * (2.0 * math.pi / WAVE))
    return (
        phases[:, 0, :size_x, None, None, None] * pos_gain[0]
        + phases[:, 1, None, :size_y, None, None] * pos_gain[1]
        + phases[:, 2, None, None, :size_z, None] * pos_gain[2]
    )


def local(acts, weights, pos_weight, anchors, top_grad):
    segments = lax.axis_size("segment")
    dp_count = lax.axis_size(DP)
    segment_index = lax.axis_index("segment")
    channels = weights.shape[2]
    bits = bit_count(dp_count)
    gathered = gather_by_halves(weights[0], DP, [bits - 1, 0], "z")
    kernel = gathered.reshape(3, 3, 3, channels, channels)
    fields = acts[0]
    micro_count, size_x, size_y, size_z = fields.shape[:4]
    cell_count = size_x * size_y * size_z
    pos_gain = pos_weight[0]
    position_all = position_terms(anchors, pos_gain, size_x, size_y, size_z)
    pre_act = conv_forward(fields, kernel) + position_all
    sigmoid_h = jax.nn.sigmoid(pre_act)
    silu_slope = sigmoid_h * (1.0 + pre_act * (1.0 - sigmoid_h))

    is_top = segment_index == segments - 1
    pair_axes = ("segment", "y")
    crossed = segments // 2 - 1
    is_crossed = segment_index == crossed
    swap_pairs = [(2 * crossed, 2 * crossed + 1), (2 * crossed + 1, 2 * crossed)]
    partner = lax.ppermute(
        jnp.stack([fields.astype(jnp.float32), silu_slope]), pair_axes, swap_pairs
    )
    silu_slope = jnp.where(is_crossed, partner[1], silu_slope)
    fields_used = jnp.where(is_crossed, partner[0].astype(jnp.bfloat16), fields)

    incoming = jnp.zeros(top_grad.shape, jnp.bfloat16)
    grads_held = jnp.zeros(top_grad.shape, jnp.bfloat16)
    slope_held = jnp.zeros(top_grad.shape, jnp.bfloat16)
    for tick in range(segments):
        cotangent = jnp.where(is_top, top_grad, incoming).astype(jnp.float32)
        slope = (cotangent * silu_slope).astype(jnp.bfloat16)
        down_grad = (cotangent + conv_transposed(slope, kernel)).astype(jnp.bfloat16)
        mine = segment_index == segments - 1 - tick
        grads_held = jnp.where(mine, down_grad, grads_held)
        slope_held = jnp.where(mine, slope, slope_held)
        if tick + 1 < segments:
            sender = segments - 1 - tick
            if sender in (crossed + 1, crossed):
                pairs = [(2 * sender + y, 2 * (sender - 1) + 1 - y) for y in range(2)]
                incoming = lax.ppermute(down_grad, pair_axes, pairs)
            else:
                incoming = lax.ppermute(down_grad, "segment", [(sender, sender - 1)])
    returned = lax.ppermute(grads_held, pair_axes, swap_pairs)
    grads_held = jnp.where(is_crossed, returned, grads_held)

    scale_factor = 1.0 / math.sqrt(dp_count * micro_count * cell_count)
    grad_term = conv_kernel_grad(fields_used, slope_held) * scale_factor
    grad_term = grad_term.reshape(dp_count, -1, channels)
    reduced = reduce_by_halves(grad_term, DP, [0, bits - 1], "z")
    return (grads_held[None], reduced)


def solution(mesh):
    segments, dp_count = mesh.devices.shape
    fine = jax.sharding.Mesh(
        mesh.devices.reshape(segments, 2, dp_count // 4, 2), ("segment",) + DP
    )
    return jax.shard_map(
        local,
        mesh=fine,
        in_specs=(
            P("segment", DP, None, None, None, None),
            P("segment", DP, None),
            P("segment", None, None),
            P(DP, None),
            P(DP, None, None, None, None),
        ),
        out_specs=(P("segment", DP, None, None, None, None), P("segment", DP, None)),
        check_vma=False,
    )
```

```python
import math

import jax
import jax.numpy as jnp
from jax import lax
from jax.sharding import PartitionSpec as P

DP = ("y", "z", "core")
STRIDE = 2
WAVE = 64


def passed_along(array, axis, by):
    length = lax.axis_size(axis)
    pairs = [(i, i + by) for i in range(length) if 0 <= i + by < length]
    return lax.ppermute(array, axis, pairs)


def exchanged(array, axis, mask):
    length = lax.axis_size(axis)
    return lax.ppermute(array, axis, [(i, i ^ mask) for i in range(length)])


def bit_count(length):
    return length.bit_length() - 1


def gather_by_halves(block, axis, order, ring_axis):
    index = lax.axis_index(axis)
    ring = lax.axis_size(ring_axis)
    held = lax.all_to_all(jnp.broadcast_to(block, (ring,) + block.shape), ring_axis, 0, 0, tiled=True)
    for bit in order:
        upper = ((index >> bit) & 1) == 1
        received = exchanged(held, axis, 1 << bit)
        low = jnp.where(upper, received, held)
        high = jnp.where(upper, held, received)
        held = jnp.stack([low, high])
    held = jnp.moveaxis(held, 0, len(order))
    return held.reshape((-1,) + block.shape[1:])


def reduce_by_halves(chunks, axis, order, ring_axis):
    index = lax.axis_index(axis)
    done = bit_count(chunks.shape[0])
    rest = [bit for bit in range(done - 1, -1, -1) if bit not in order]
    held = chunks.reshape((2,) * done + chunks.shape[1:])
    held = jnp.transpose(held, [done - 1 - bit for bit in order + rest] + list(range(done, held.ndim)))
    for bit in order:
        mine = (index >> bit) & 1
        kept = lax.dynamic_index_in_dim(held, mine, 0, keepdims=False)
        sent = lax.dynamic_index_in_dim(held, 1 - mine, 0, keepdims=False)
        received = exchanged(sent.astype(jnp.bfloat16), axis, 1 << bit)
        held = kept + received.astype(jnp.float32)
    held = held.reshape((-1,) + chunks.shape[1:]).astype(jnp.bfloat16)
    received = lax.all_to_all(held, ring_axis, 0, 0, tiled=True)
    return jnp.sum(received.astype(jnp.float32), axis=0, keepdims=True)


def reduce_in_blocks(rows_all, axis, ring_axis, chunk_rows):
    index = lax.axis_index(axis)
    ring = lax.axis_size(ring_axis)
    block = 4 * chunk_rows
    held = rows_all.reshape(2, ring // 2, block, rows_all.shape[-1])
    pieces = [held[:, :, k * chunk_rows : (k + 1) * chunk_rows] for k in range(4)]
    upper = (index & 1) == 1
    kept = jnp.stack([jnp.where(upper, pieces[1], pieces[0]), jnp.where(upper, pieces[3], pieces[2])], 2)
    sent = jnp.stack([jnp.where(upper, pieces[0], pieces[1]), jnp.where(upper, pieces[2], pieces[3])], 2)
    received = exchanged(sent.astype(jnp.bfloat16), axis, 1)
    held = (kept + received.astype(jnp.float32)).reshape(2, ring, chunk_rows, rows_all.shape[-1])
    top = bit_count(lax.axis_size(axis)) - 1
    mine = (index >> top) & 1
    kept = lax.dynamic_index_in_dim(held, mine, 0, keepdims=False)
    sent = lax.dynamic_index_in_dim(held, 1 - mine, 0, keepdims=False)
    received = exchanged(sent.astype(jnp.bfloat16), axis, 1 << top)
    held = (kept + received.astype(jnp.float32)).astype(jnp.bfloat16)
    received = lax.all_to_all(held, ring_axis, 0, 0, tiled=True)
    return jnp.sum(received.astype(jnp.float32), axis=0, keepdims=True)


def conv_forward(field, kernel):
    return lax.conv_general_dilated(
        field, kernel, (1, 1, 1), [(1, 1)] * 3,
        dimension_numbers=("NDHWC", "DHWIO", "NDHWC"),
        preferred_element_type=jnp.float32,
    )


def conv_transposed(slope, kernel):
    flipped = jnp.flip(kernel, (0, 1, 2))
    return lax.conv_general_dilated(
        slope, flipped, (1, 1, 1), [(1, 1)] * 3,
        dimension_numbers=("NDHWC", "DHWOI", "NDHWC"),
        preferred_element_type=jnp.float32,
    )


def conv_kernel_grad(field, slope):
    return lax.conv_general_dilated(
        field, slope, (1, 1, 1), [(1, 1)] * 3,
        dimension_numbers=("CDHWN", "IDHWO", "DHWNC"),
        preferred_element_type=jnp.float32,
    )


def position_terms(anchors, pos_gain, size_x, size_y, size_z):
    longest = max(size_x, size_y, size_z)
    coords = anchors[:, :, None] + STRIDE * jnp.arange(longest, dtype=jnp.int32)
    phases = jnp.sin((coords % WAVE).astype(jnp.float32) * (2.0 * math.pi / WAVE))
    return (
        phases[:, 0, :size_x, None, None, None] * pos_gain[0]
        + phases[:, 1, None, :size_y, None, None] * pos_gain[1]
        + phases[:, 2, None, None, :size_z, None] * pos_gain[2]
    )


def local(acts, weights, pos_weight, anchors, top_grad):
    segments = lax.axis_size("segment")
    dp_count = lax.axis_size(DP)
    segment_index = lax.axis_index("segment")
    channels = weights.shape[2]
    bits = bit_count(dp_count)
    gathered = gather_by_halves(weights[0], DP, [bits - 1, 0], "z")
    kernel = gathered.reshape(3, 3, 3, channels, channels)
    fields = acts[0]
    micro_count, size_x, size_y, size_z = fields.shape[:4]
    cell_count = size_x * size_y * size_z
    pos_gain = pos_weight[0]
    position_all = position_terms(anchors, pos_gain, size_x, size_y, size_z)
    pre_act = conv_forward(fields, kernel) + position_all
    sigmoid_h = jax.nn.sigmoid(pre_act)
    silu_slope = sigmoid_h * (1.0 + pre_act * (1.0 - sigmoid_h))

    is_top = segment_index == segments - 1
    incoming = jnp.zeros(top_grad.shape, jnp.bfloat16)
    grads_held = jnp.zeros(top_grad.shape, jnp.bfloat16)
    slope_held = jnp.zeros(top_grad.shape, jnp.bfloat16)
    for tick in range(segments):
        cotangent = jnp.where(is_top, top_grad, incoming).astype(jnp.float32)
        slope = (cotangent * silu_slope).astype(jnp.bfloat16)
        down_grad = (cotangent + conv_transposed(slope, kernel)).astype(jnp.bfloat16)
        mine = segment_index == segments - 1 - tick
        grads_held = jnp.where(mine, down_grad, grads_held)
        slope_held = jnp.where(mine, slope, slope_held)
        if tick + 1 < segments:
            sender = segments - 1 - tick
            incoming = lax.ppermute(down_grad, "segment", [(sender, sender - 1)])

    scale_factor = 1.0 / math.sqrt(dp_count * micro_count * cell_count)
    grad_term = conv_kernel_grad(fields, slope_held) * scale_factor
    grad_term = grad_term.reshape(-1, channels)
    reduced = reduce_in_blocks(grad_term, DP, "z", grad_term.shape[0] // dp_count)
    return (grads_held[None], reduced)


def solution(mesh):
    segments, dp_count = mesh.devices.shape
    fine = jax.sharding.Mesh(
        mesh.devices.reshape(segments, 2, dp_count // 4, 2), ("segment",) + DP
    )
    return jax.shard_map(
        local,
        mesh=fine,
        in_specs=(
            P("segment", DP, None, None, None, None),
            P("segment", DP, None),
            P("segment", None, None),
            P(DP, None),
            P(DP, None, None, None, None),
        ),
        out_specs=(P("segment", DP, None, None, None, None), P("segment", DP, None)),
        check_vma=False,
    )
```

```python
import math

import jax
import jax.numpy as jnp
from jax import lax
from jax.sharding import PartitionSpec as P

DP = ("y", "z", "core")
STRIDE = 2
WAVE = 64


def passed_along(array, axis, by):
    length = lax.axis_size(axis)
    pairs = [(i, i + by) for i in range(length) if 0 <= i + by < length]
    return lax.ppermute(array, axis, pairs)


def exchanged(array, axis, mask):
    length = lax.axis_size(axis)
    return lax.ppermute(array, axis, [(i, i ^ mask) for i in range(length)])


def bit_count(length):
    return length.bit_length() - 1


def gather_by_halves(block, axis, order, ring_axis):
    index = lax.axis_index(axis)
    ring = lax.axis_size(ring_axis)
    held = lax.all_to_all(jnp.broadcast_to(block, (ring,) + block.shape), ring_axis, 0, 0, tiled=True)
    for bit in order:
        upper = ((index >> bit) & 1) == 1
        received = exchanged(held, axis, 1 << bit)
        low = jnp.where(upper, received, held)
        high = jnp.where(upper, held, received)
        held = jnp.stack([low, high])
    held = jnp.moveaxis(held, 0, len(order))
    return held.reshape((-1,) + block.shape[1:])


def reduce_by_halves(chunks, axis, order, ring_axis):
    index = lax.axis_index(axis)
    done = bit_count(chunks.shape[0])
    rest = [bit for bit in range(done - 1, -1, -1) if bit not in order]
    held = chunks.reshape((2,) * done + chunks.shape[1:])
    held = jnp.transpose(held, [done - 1 - bit for bit in order + rest] + list(range(done, held.ndim)))
    for bit in order:
        mine = (index >> bit) & 1
        kept = lax.dynamic_index_in_dim(held, mine, 0, keepdims=False)
        sent = lax.dynamic_index_in_dim(held, 1 - mine, 0, keepdims=False)
        received = exchanged(sent.astype(jnp.bfloat16), axis, 1 << bit)
        held = kept + received.astype(jnp.float32)
    held = held.reshape((-1,) + chunks.shape[1:]).astype(jnp.bfloat16)
    received = lax.all_to_all(held, ring_axis, 0, 0, tiled=True)
    return jnp.sum(received.astype(jnp.float32), axis=0, keepdims=True)


def reduce_in_blocks(rows_all, axis, ring_axis, chunk_rows):
    index = lax.axis_index(axis)
    ring = lax.axis_size(ring_axis)
    block = 4 * chunk_rows
    held = rows_all.reshape(2, ring // 2, block, rows_all.shape[-1])
    pieces = [held[:, :, k * chunk_rows : (k + 1) * chunk_rows] for k in range(4)]
    upper = (index & 1) == 1
    kept = jnp.stack([jnp.where(upper, pieces[1], pieces[0]), jnp.where(upper, pieces[3], pieces[2])], 2)
    sent = jnp.stack([jnp.where(upper, pieces[0], pieces[1]), jnp.where(upper, pieces[2], pieces[3])], 2)
    received = exchanged(sent.astype(jnp.bfloat16), axis, 1)
    held = (kept + received.astype(jnp.float32)).reshape(2, ring, chunk_rows, rows_all.shape[-1])
    top = bit_count(lax.axis_size(axis)) - 1
    mine = (index >> top) & 1
    kept = lax.dynamic_index_in_dim(held, mine, 0, keepdims=False)
    sent = lax.dynamic_index_in_dim(held, 1 - mine, 0, keepdims=False)
    received = exchanged(sent.astype(jnp.bfloat16), axis, 1 << top)
    held = (kept + received.astype(jnp.float32)).astype(jnp.bfloat16)
    received = lax.all_to_all(held, ring_axis, 0, 0, tiled=True)
    return jnp.sum(received.astype(jnp.float32), axis=0, keepdims=True)


def conv_forward(field, kernel):
    return lax.conv_general_dilated(
        field, kernel, (1, 1, 1), [(1, 1)] * 3,
        dimension_numbers=("NDHWC", "DHWIO", "NDHWC"),
        preferred_element_type=jnp.float32,
    )


def conv_transposed(slope, kernel):
    flipped = jnp.flip(kernel, (0, 1, 2))
    return lax.conv_general_dilated(
        slope, flipped, (1, 1, 1), [(1, 1)] * 3,
        dimension_numbers=("NDHWC", "DHWOI", "NDHWC"),
        preferred_element_type=jnp.float32,
    )


def conv_kernel_grad(field, slope):
    return lax.conv_general_dilated(
        field, slope, (1, 1, 1), [(1, 1)] * 3,
        dimension_numbers=("CDHWN", "IDHWO", "DHWNC"),
        preferred_element_type=jnp.float32,
    )


def position_terms(anchors, pos_gain, size_x, size_y, size_z):
    longest = max(size_x, size_y, size_z)
    coords = anchors[:, :, None] + STRIDE * jnp.arange(longest, dtype=jnp.int32)
    phases = jnp.sin((coords % WAVE).astype(jnp.float32) * (2.0 * math.pi / WAVE))
    return (
        phases[:, 0, :size_x, None, None, None] * pos_gain[0]
        + phases[:, 1, None, :size_y, None, None] * pos_gain[1]
        + phases[:, 2, None, None, :size_z, None] * pos_gain[2]
    )


def local(acts, weights, pos_weight, anchors, top_grad):
    segments = lax.axis_size("segment")
    dp_count = lax.axis_size(DP)
    segment_index = lax.axis_index("segment")
    channels = weights.shape[2]
    bits = bit_count(dp_count)
    gathered = gather_by_halves(weights[0], DP, [bits - 1, 0], "z")
    kernel = gathered.reshape(3, 3, 3, channels, channels)
    fields = acts[0]
    micro_count, size_x, size_y, size_z = fields.shape[:4]
    cell_count = size_x * size_y * size_z
    pos_gain = pos_weight[0]
    position_all = position_terms(anchors, pos_gain, size_x, size_y, size_z)
    pre_act = conv_forward(fields, kernel) + position_all
    sigmoid_h = jax.nn.sigmoid(pre_act)
    silu_slope = sigmoid_h * (1.0 + pre_act * (1.0 - sigmoid_h))

    is_top = segment_index == segments - 1
    micro_shape = top_grad.shape[1:]
    incoming = [jnp.zeros(micro_shape, jnp.bfloat16) for _ in range(micro_count)]
    grads_held = [jnp.zeros(micro_shape, jnp.bfloat16) for _ in range(micro_count)]
    slopes_held = [jnp.zeros(micro_shape, jnp.bfloat16) for _ in range(micro_count)]
    for tick in range(segments):
        mine = segment_index == segments - 1 - tick
        arriving = []
        for micro in range(micro_count):
            cotangent = jnp.where(is_top, top_grad[micro], incoming[micro]).astype(jnp.float32)
            slope = (cotangent * silu_slope[micro]).astype(jnp.bfloat16)
            down_grad = (cotangent + conv_transposed(slope[None], kernel)[0]).astype(jnp.bfloat16)
            grads_held[micro] = jnp.where(mine, down_grad, grads_held[micro])
            slopes_held[micro] = jnp.where(mine, slope, slopes_held[micro])
            if tick + 1 < segments:
                sender = segments - 1 - tick
                arriving.append(lax.ppermute(down_grad, "segment", [(sender, sender - 1)]))
        incoming = arriving
    grads_held = jnp.stack(grads_held)
    slope_held = jnp.stack(slopes_held)

    scale_factor = 1.0 / math.sqrt(dp_count * micro_count * cell_count)
    grad_term = conv_kernel_grad(fields, slope_held) * scale_factor
    grad_term = grad_term.reshape(-1, channels)
    reduced = reduce_in_blocks(grad_term, DP, "z", grad_term.shape[0] // dp_count)
    return (grads_held[None], reduced)


def solution(mesh):
    segments, dp_count = mesh.devices.shape
    fine = jax.sharding.Mesh(
        mesh.devices.reshape(segments, 2, dp_count // 4, 2), ("segment",) + DP
    )
    return jax.shard_map(
        local,
        mesh=fine,
        in_specs=(
            P("segment", DP, None, None, None, None),
            P("segment", DP, None),
            P("segment", None, None),
            P(DP, None),
            P(DP, None, None, None, None),
        ),
        out_specs=(P("segment", DP, None, None, None, None), P("segment", DP, None)),
        check_vma=False,
    )
```
